512 devices in a mesh: fibre: 32 (over z, core), group: 16 (over y, x).
Axes of the slice: x: 4, y: 4, z: 16, core: 2. Of those that a mesh axis runs over, the one named last changes fastest.
Arguments:
- species_field: float32 [512, 524288], P('fibre', 'group'), may hold values from -45 to 45, as said below
- start_block: float32 [512, 64], replicated, may hold values from -4 to 4
Outputs:
- mode_basis: float32 [512, 64], replicated
- core_tensor: float32 [64, 524288], P(None, ('group', 'fibre'))
The draws below stay inside these ranges and needn't reach their ends.
Inputs may be any that keep to these rules, and one draw needn't show every extreme that they name: `species_field`: float32 field values.
All inputs are finite; a program needn't handle non-finite values.
Results may differ from the reference program's by a relative error of at most 0.0003.
Values sent between devices are 32-bit elements; how exact they have to be, the bound alone decides.
No kernel may reach another device: no remote copies, remote signals or barrier semaphores. Data moves between devices by JAX's collectives and lax.ppermute only.
A program may use at most 64 MiB of HBM per device.

```python
import math
import jax
import jax.numpy as jnp
from jax import lax

I1 = 512
RANK = 64
ITERS = 3
COLS = 524288


def draw_species_field(key, part):
    keys = jax.random.split(key, 5)
    noise_draw = jax.random.truncated_normal(keys[0], -4.0, 4.0, (I1, COLS), jnp.float32)
    common_scale = 0.15
    upper_log = math.log(3.0)
    row_order = jax.random.permutation(keys[1], I1)
    mixed_noise = noise_draw + 0.6 * noise_draw[row_order]
    row_logs = jax.random.uniform(keys[2], (I1, 1), jnp.float32, 0.0, upper_log)
    position = jnp.arange(COLS, dtype=jnp.float32) / COLS
    amplitude = jnp.exp(row_logs * (2.0 * position[None, :] - 1.0)) * (0.6 + 1.2 * position[None, :])
    common_row = jax.random.truncated_normal(keys[3], -4.0, 4.0, (1, COLS), jnp.float32)
    common_weight = common_scale * jax.random.truncated_normal(keys[4], -4.0, 4.0, (I1, 1), jnp.float32)
    return (amplitude * mixed_noise + common_weight * common_row).astype(jnp.float32)


def noise(stream_key, shape, deviation, reach, kind=jnp.bfloat16):
    values = jax.random.normal(stream_key, shape, jnp.float32) * deviation
    return jnp.minimum(jnp.maximum(values, -reach), reach).astype(kind)


def setup_inputs(seed: int = 0) -> dict:
    key_of = jax.random.split(jax.random.key(seed), 3)
    species_field = draw_species_field(jax.random.fold_in(key_of[2], 71), 0)
    start_block = noise(key_of[1], (I1, RANK), 1.0, 4.0, jnp.float32)
    return dict(species_field=species_field, start_block=start_block)


highest_precision = lax.Precision.HIGHEST

def orthonormal(matrix):
    inner_gram = jnp.dot(matrix.T, matrix, precision=highest_precision)
    lower_factor = jnp.linalg.cholesky(inner_gram)
    return lax.linalg.triangular_solve(lower_factor, matrix, left_side=False, lower=True, transpose_a=True)

def reference(species_field, start_block):
    gram_matrix = jnp.dot(species_field, species_field.T, precision=highest_precision) / COLS
    mode_basis = orthonormal(start_block)
    for iteration in range(ITERS):
        mode_basis = orthonormal(jnp.dot(gram_matrix, mode_basis, precision=highest_precision))
    core_tensor = jnp.dot(mode_basis.T, species_field, precision=highest_precision)
    return (mode_basis, core_tensor)
```

```python
import jax
import jax.numpy as jnp
from jax import lax
from jax.sharding import PartitionSpec as P

ITERS = 3


highest_precision = lax.Precision.HIGHEST


def orthonormal(matrix):
    inner_gram = jnp.dot(matrix.T, matrix, precision=highest_precision)
    lower_factor = jnp.linalg.cholesky(inner_gram)
    return lax.linalg.triangular_solve(
        lower_factor, matrix, left_side=False, lower=True, transpose_a=True
    )


def exchange(blocks, axis):
    return lax.all_to_all(blocks, axis, 0, 0, tiled=True)


def reduce_scatter(matrix, axis):
    parts = lax.axis_size(axis)
    blocks = matrix.reshape(parts, matrix.shape[0] // parts, *matrix.shape[1:])
    return exchange(blocks, axis).sum(0)


def gather(matrix, axis):
    parts = lax.axis_size(axis)
    blocks = jnp.broadcast_to(matrix[None], (parts,) + matrix.shape)
    return exchange(blocks, axis).reshape(parts * matrix.shape[0], *matrix.shape[1:])


def all_reduce(matrix):
    rows = reduce_scatter(matrix, "group")
    rows = reduce_scatter(rows, "fibre")
    rows = gather(rows, "fibre")
    return gather(rows, "group")


def on_device(species_field, start_block):
    fibres = lax.all_to_all(species_field, "fibre", split_axis=1, concat_axis=0, tiled=True)
    total_columns = fibres.shape[1] * lax.axis_size("fibre") * lax.axis_size("group")
    mode_basis = orthonormal(start_block)
    local_gram = jnp.dot(fibres, fibres.T, precision=highest_precision) / total_columns
    gram_matrix = all_reduce(local_gram)
    for iteration in range(ITERS):
        mode_basis = orthonormal(jnp.dot(gram_matrix, mode_basis, precision=highest_precision))
    core_tensor = jnp.dot(mode_basis.T, fibres, precision=highest_precision)
    return (mode_basis, core_tensor)


def solution(mesh):
    placed = (P("fibre", "group"), P())
    return jax.shard_map(
        on_device,
        mesh=mesh,
        in_specs=placed,
        out_specs=(P(), P(None, ("group", "fibre"))),
        check_vma=False,
    )
```

```python
import jax
import jax.numpy as jnp
from jax import lax
from jax.experimental import pallas as pl
from jax.sharding import PartitionSpec as P

ITERS = 3


highest_precision = lax.Precision.HIGHEST


def inverse_cholesky_kernel(inner_ref, inverse_ref):
    size = inner_ref.shape[0]
    schur = inner_ref[...]
    rows = lax.broadcasted_iota(jnp.int32, (size, 1), 0)
    cols = lax.broadcasted_iota(jnp.int32, (1, size), 1)
    inverse = (rows == cols).astype(jnp.float32)
    for j in range(size):
        inv_pivot = lax.rsqrt(schur[j:j + 1, j:j + 1])
        factor_col = jnp.where(rows >= j, schur[:, j:j + 1] * inv_pivot, 0.0)
        factor_row = jnp.where(cols >= j, schur[j:j + 1, :] * inv_pivot, 0.0)
        schur = schur - factor_col * factor_row
        step = jnp.where(rows > j, factor_col * inv_pivot, jnp.where(rows == j, 1.0 - inv_pivot, 0.0))
        inverse = inverse - step * inverse[j:j + 1, :]
    inverse_ref[...] = inverse


def inverse_cholesky(inner_gram):
    return pl.pallas_call(
        inverse_cholesky_kernel,
        out_shape=jax.ShapeDtypeStruct(inner_gram.shape, jnp.float32),
    )(inner_gram)


def orthonormal(matrix):
    inner_gram = jnp.dot(matrix.T, matrix, precision=highest_precision)
    lower_inverse = inverse_cholesky(inner_gram)
    return lax.dot_general(
        matrix, lower_inverse, (((1,), (1,)), ((), ())), precision=highest_precision
    )


def exchange(blocks, axis):
    return lax.all_to_all(blocks, axis, 0, 0, tiled=True)


def reduce_scatter(matrix, axis):
    parts = lax.axis_size(axis)
    blocks = matrix.reshape(parts, matrix.shape[0] // parts, *matrix.shape[1:])
    return exchange(blocks, axis).sum(0)


def gather(matrix, axis):
    parts = lax.axis_size(axis)
    blocks = jnp.broadcast_to(matrix[None], (parts,) + matrix.shape)
    return exchange(blocks, axis).reshape(parts * matrix.shape[0], *matrix.shape[1:])


def all_reduce(matrix):
    rows = reduce_scatter(matrix, "group")
    rows = reduce_scatter(rows, "fibre")
    rows = gather(rows, "fibre")
    return gather(rows, "group")


def on_device(species_field, start_block):
    fibres = lax.all_to_all(species_field, "fibre", split_axis=1, concat_axis=0, tiled=True)
    total_columns = fibres.shape[1] * lax.axis_size("fibre") * lax.axis_size("group")
    mode_basis = orthonormal(start_block)
    local_gram = jnp.dot(fibres, fibres.T, precision=highest_precision) / total_columns
    gram_matrix = all_reduce(local_gram)
    for iteration in range(ITERS):
        mode_basis = orthonormal(jnp.dot(gram_matrix, mode_basis, precision=highest_precision))
    core_tensor = jnp.dot(mode_basis.T, fibres, precision=highest_precision)
    return (mode_basis, core_tensor)


def solution(mesh):
    placed = (P("fibre", "group"), P())
    return jax.shard_map(
        on_device,
        mesh=mesh,
        in_specs=placed,
        out_specs=(P(), P(None, ("group", "fibre"))),
        check_vma=False,
    )
```

```python
import jax
import jax.numpy as jnp
from jax import lax
from jax.experimental import pallas as pl
from jax.sharding import PartitionSpec as P

ITERS = 3


highest_precision = lax.Precision.HIGHEST


def inverse_cholesky(inner_gram):
    size = inner_gram.shape[0]
    schur = inner_gram
    rows = lax.broadcasted_iota(jnp.int32, (size, 1), 0)
    cols = lax.broadcasted_iota(jnp.int32, (1, size), 1)
    inverse = (rows == cols).astype(jnp.float32)
    for j in range(size):
        inv_pivot = lax.rsqrt(schur[j:j + 1, j:j + 1])
        factor_col = jnp.where(rows >= j, schur[:, j:j + 1] * inv_pivot, 0.0)
        factor_row = jnp.where(cols >= j, schur[j:j + 1, :] * inv_pivot, 0.0)
        schur = schur - factor_col * factor_row
        step = jnp.where(rows > j, factor_col * inv_pivot, jnp.where(rows == j, 1.0 - inv_pivot, 0.0))
        inverse = inverse - step * inverse[j:j + 1, :]
    return inverse


def orthonormal_in_kernel(matrix):
    inner_gram = jnp.dot(matrix.T, matrix, precision=highest_precision,
                         preferred_element_type=jnp.float32)
    lower_inverse = inverse_cholesky(inner_gram)
    return lax.dot_general(
        matrix, lower_inverse, (((1,), (1,)), ((), ())), precision=highest_precision,
        preferred_element_type=jnp.float32,
    )


def orthonormal_kernel(block_ref, basis_ref):
    basis_ref[...] = orthonormal_in_kernel(block_ref[...])


def iterate_kernel(gram_ref, basis_ref, out_ref):
    basis = basis_ref[...]
    for iteration in range(ITERS):
        product = jnp.dot(gram_ref[...], basis, precision=highest_precision,
                          preferred_element_type=jnp.float32)
        basis = orthonormal_in_kernel(product)
    out_ref[...] = basis


def orthonormal(matrix):
    return pl.pallas_call(
        orthonormal_kernel,
        out_shape=jax.ShapeDtypeStruct(matrix.shape, jnp.float32),
    )(matrix)


def subspace_iteration(gram_matrix, mode_basis):
    return pl.pallas_call(
        iterate_kernel,
        out_shape=jax.ShapeDtypeStruct(mode_basis.shape, jnp.float32),
    )(gram_matrix, mode_basis)


def exchange(blocks, axis):
    return lax.all_to_all(blocks, axis, 0, 0, tiled=True)


def reduce_scatter(matrix, axis):
    parts = lax.axis_size(axis)
    blocks = matrix.reshape(parts, matrix.shape[0] // parts, *matrix.shape[1:])
    return exchange(blocks, axis).sum(0)


def gather(matrix, axis):
    parts = lax.axis_size(axis)
    blocks = jnp.broadcast_to(matrix[None], (parts,) + matrix.shape)
    return exchange(blocks, axis).reshape(parts * matrix.shape[0], *matrix.shape[1:])


def all_reduce(matrix):
    rows = reduce_scatter(matrix, "group")
    rows = reduce_scatter(rows, "fibre")
    rows = gather(rows, "fibre")
    return gather(rows, "group")


def on_device(species_field, start_block):
    fibres = lax.all_to_all(species_field, "fibre", split_axis=1, concat_axis=0, tiled=True)
    total_columns = fibres.shape[1] * lax.axis_size("fibre") * lax.axis_size("group")
    mode_basis = orthonormal(start_block)
    local_gram = jnp.dot(fibres, fibres.T, precision=highest_precision) / total_columns
    gram_matrix = all_reduce(local_gram)
    mode_basis = subspace_iteration(gram_matrix, mode_basis)
    core_tensor = jnp.dot(mode_basis.T, fibres, precision=highest_precision)
    return (mode_basis, core_tensor)


def solution(mesh):
    placed = (P("fibre", "group"), P())
    return jax.shard_map(
        on_device,
        mesh=mesh,
        in_specs=placed,
        out_specs=(P(), P(None, ("group", "fibre"))),
        check_vma=False,
    )
```

```python
import jax
import jax.numpy as jnp
from jax import lax
from jax.experimental import pallas as pl
from jax.sharding import PartitionSpec as P

ITERS = 3


highest_precision = lax.Precision.HIGHEST


def inverse_cholesky(inner_gram):
    size = inner_gram.shape[0]
    schur = inner_gram
    rows = lax.broadcasted_iota(jnp.int32, (size, 1), 0)
    cols = lax.broadcasted_iota(jnp.int32, (1, size), 1)
    inverse = (rows == cols).astype(jnp.float32)
    for j in range(size):
        inv_pivot = lax.rsqrt(schur[j:j + 1, j:j + 1])
        factor_col = jnp.where(rows >= j, schur[:, j:j + 1] * inv_pivot, 0.0)
        factor_row = jnp.where(cols >= j, schur[j:j + 1, :] * inv_pivot, 0.0)
        schur = schur - factor_col * factor_row
        step = jnp.where(rows > j, factor_col * inv_pivot, jnp.where(rows == j, 1.0 - inv_pivot, 0.0))
        inverse = inverse - step * inverse[j:j + 1, :]
    return inverse


def orthonormal_in_kernel(matrix):
    inner_gram = jnp.dot(matrix.T, matrix, precision=highest_precision,
                         preferred_element_type=jnp.float32)
    lower_inverse = inverse_cholesky(inner_gram)
    return lax.dot_general(
        matrix, lower_inverse, (((1,), (1,)), ((), ())), precision=highest_precision,
        preferred_element_type=jnp.float32,
    )


def orthonormal_kernel(block_ref, basis_ref):
    basis_ref[...] = orthonormal_in_kernel(block_ref[...])


def iterate_kernel(gram_ref, basis_ref, out_ref):
    basis = basis_ref[...]
    for iteration in range(ITERS):
        product = jnp.dot(gram_ref[...], basis, precision=highest_precision,
                          preferred_element_type=jnp.float32)
        basis = orthonormal_in_kernel(product)
    out_ref[...] = basis


def orthonormal(matrix):
    return pl.pallas_call(
        orthonormal_kernel,
        out_shape=jax.ShapeDtypeStruct(matrix.shape, jnp.float32),
    )(matrix)


def subspace_iteration(gram_matrix, mode_basis):
    return pl.pallas_call(
        iterate_kernel,
        out_shape=jax.ShapeDtypeStruct(mode_basis.shape, jnp.float32),
    )(gram_matrix, mode_basis)


def exchange(blocks, axis):
    return lax.all_to_all(blocks, axis, 0, 0, tiled=True)


def reduce_scatter(matrix, axis):
    parts = lax.axis_size(axis)
    blocks = matrix.reshape(parts, matrix.shape[0] // parts, *matrix.shape[1:])
    return exchange(blocks, axis).sum(0)


def gather(matrix, axis):
    parts = lax.axis_size(axis)
    blocks = jnp.broadcast_to(matrix[None], (parts,) + matrix.shape)
    return exchange(blocks, axis).reshape(parts * matrix.shape[0], *matrix.shape[1:])


def all_reduce(matrix):
    rows = reduce_scatter(matrix, "group")
    rows = reduce_scatter(rows, "fibre")
    rows = gather(rows, "fibre")
    return gather(rows, "group")


def on_device(species_field, start_block):
    fibres = lax.all_to_all(species_field, "fibre", split_axis=1, concat_axis=0, tiled=True)
    total_columns = fibres.shape[1] * lax.axis_size("fibre") * lax.axis_size("group")
    fibres, mode_basis = lax.optimization_barrier((fibres, orthonormal(start_block)))
    local_gram = jnp.dot(fibres, fibres.T, precision=highest_precision) / total_columns
    gram_matrix = all_reduce(local_gram)
    mode_basis = subspace_iteration(gram_matrix, mode_basis)
    core_tensor = jnp.dot(mode_basis.T, fibres, precision=highest_precision)
    return (mode_basis, core_tensor)


def solution(mesh):
    placed = (P("fibre", "group"), P())
    return jax.shard_map(
        on_device,
        mesh=mesh,
        in_specs=placed,
        out_specs=(P(), P(None, ("group", "fibre"))),
        check_vma=False,
    )
```

```python
import jax
import jax.numpy as jnp
from jax import lax
from jax.experimental import pallas as pl
from jax.sharding import PartitionSpec as P

ITERS = 3


highest_precision = lax.Precision.HIGHEST


def inverse_cholesky(inner_gram):
    size = inner_gram.shape[0]
    schur = inner_gram
    rows = lax.broadcasted_iota(jnp.int32, (size, 1), 0)
    cols = lax.broadcasted_iota(jnp.int32, (1, size), 1)
    inverse = (rows == cols).astype(jnp.float32)
    for j in range(size):
        inv_pivot = lax.rsqrt(schur[j:j + 1, j:j + 1])
        factor_col = jnp.where(rows >= j, schur[:, j:j + 1] * inv_pivot, 0.0)
        factor_row = jnp.where(cols >= j, schur[j:j + 1, :] * inv_pivot, 0.0)
        schur = schur - factor_col * factor_row
        step = jnp.where(rows > j, factor_col * inv_pivot, jnp.where(rows == j, 1.0 - inv_pivot, 0.0))
        inverse = inverse - step * inverse[j:j + 1, :]
    return inverse


def orthonormal_in_kernel(matrix):
    inner_gram = jnp.dot(matrix.T, matrix, precision=highest_precision,
                         preferred_element_type=jnp.float32)
    lower_inverse = inverse_cholesky(inner_gram)
    return lax.dot_general(
        matrix, lower_inverse, (((1,), (1,)), ((), ())), precision=highest_precision,
        preferred_element_type=jnp.float32,
    )


def orthonormal_kernel(block_ref, basis_ref):
    basis_ref[...] = orthonormal_in_kernel(block_ref[...])


def iterate_kernel(gram_ref, basis_ref, out_ref):
    basis = basis_ref[...]
    for iteration in range(ITERS):
        product = jnp.dot(gram_ref[...], basis, precision=highest_precision,
                          preferred_element_type=jnp.float32)
        basis = orthonormal_in_kernel(product)
    out_ref[...] = basis


def orthonormal(matrix):
    return pl.pallas_call(
        orthonormal_kernel,
        out_shape=jax.ShapeDtypeStruct(matrix.shape, jnp.float32),
    )(matrix)


def subspace_iteration(gram_matrix, mode_basis):
    return pl.pallas_call(
        iterate_kernel,
        out_shape=jax.ShapeDtypeStruct(mode_basis.shape, jnp.float32),
    )(gram_matrix, mode_basis)


def exchange(blocks, axis):
    return lax.all_to_all(blocks, axis, 0, 0, tiled=True)


def reduce_scatter(matrix, axis):
    parts = lax.axis_size(axis)
    blocks = matrix.reshape(parts, matrix.shape[0] // parts, *matrix.shape[1:])
    return exchange(blocks, axis).sum(0)


def gather(matrix, axis):
    parts = lax.axis_size(axis)
    blocks = jnp.broadcast_to(matrix[None], (parts,) + matrix.shape)
    return exchange(blocks, axis).reshape(parts * matrix.shape[0], *matrix.shape[1:])


def pad_rows(matrix, rows):
    return jnp.pad(matrix, ((0, rows - matrix.shape[0]), (0, 0)))


def all_reduce(matrix):
    groups, fibres = lax.axis_size("group"), lax.axis_size("fibre")
    rows = pad_rows(matrix, -(-matrix.shape[0] // groups) * groups)
    rows = reduce_scatter(rows, "group")
    chunk = rows.shape[0]
    rows = pad_rows(rows, -(-chunk // fibres) * fibres)
    rows = reduce_scatter(rows, "fibre")
    rows = gather(rows, "fibre")[:chunk]
    return gather(rows, "group")[:matrix.shape[0]]


def pack_symmetric(gram):
    half = gram.shape[0] // 2
    upper_left, upper_right, lower_right = gram[:half, :half], gram[:half, half:], gram[half:, half:]
    index = jnp.arange(half)
    on_or_above = index[:, None] <= index[None, :]
    triangles = jnp.where(on_or_above, upper_left, lower_right)
    diagonal = jnp.diagonal(lower_right)[None, :]
    return jnp.concatenate([triangles, upper_right, diagonal], axis=0)


def unpack_symmetric(packed):
    half = packed.shape[1]
    triangles, upper_right, diagonal = packed[:half], packed[half:2 * half], packed[2 * half]
    index = jnp.arange(half)
    on_or_above = index[:, None] <= index[None, :]
    below = index[:, None] > index[None, :]
    upper_left = jnp.where(on_or_above, triangles, triangles.T)
    lower_right = jnp.where(below, triangles, triangles.T)
    lower_right = jnp.where(index[:, None] == index[None, :], diagonal[None, :], lower_right)
    return jnp.concatenate([
        jnp.concatenate([upper_left, upper_right], axis=1),
        jnp.concatenate([upper_right.T, lower_right], axis=1),
    ], axis=0)


def on_device(species_field, start_block):
    fibres = lax.all_to_all(species_field, "fibre", split_axis=1, concat_axis=0, tiled=True)
    total_columns = fibres.shape[1] * lax.axis_size("fibre") * lax.axis_size("group")
    fibres, mode_basis = lax.optimization_barrier((fibres, orthonormal(start_block)))
    local_gram = jnp.dot(fibres, fibres.T, precision=highest_precision) / total_columns
    gram_matrix = unpack_symmetric(all_reduce(pack_symmetric(local_gram)))
    mode_basis = subspace_iteration(gram_matrix, mode_basis)
    core_tensor = jnp.dot(mode_basis.T, fibres, precision=highest_precision)
    return (mode_basis, core_tensor)


def solution(mesh):
    placed = (P("fibre", "group"), P())
    return jax.shard_map(
        on_device,
        mesh=mesh,
        in_specs=placed,
        out_specs=(P(), P(None, ("group", "fibre"))),
        check_vma=False,
    )
```

```python
import jax
import jax.numpy as jnp
from jax import lax
from jax.experimental import pallas as pl
from jax.sharding import PartitionSpec as P

ITERS = 3


highest_precision = lax.Precision.HIGHEST


def inverse_cholesky(inner_gram):
    size = inner_gram.shape[0]
    count = size // 8
    schur = [inner_gram[8 * b:8 * b + 8, :] for b in range(count)]
    rows = lax.broadcasted_iota(jnp.int32, (8, 1), 0)
    cols = lax.broadcasted_iota(jnp.int32, (1, size), 1)
    inverse = [((rows + 8 * b) == cols).astype(jnp.float32) for b in range(count)]
    for j in range(size):
        pivot_block, r = divmod(j, 8)
        pivot_row = schur[pivot_block][r:r + 1, :]
        inv_pivot = lax.rsqrt(pivot_row[:, j:j + 1])
        recip = inv_pivot * inv_pivot
        scaled_row = jnp.where(cols >= j, pivot_row, 0.0) * recip
        inverse_row = inverse[pivot_block][r:r + 1, :]
        for b in range(pivot_block, count):
            col = schur[b][:, j:j + 1]
            if b == pivot_block:
                col = jnp.where(rows >= r, col, 0.0)
                step = jnp.where(rows > r, col * recip, jnp.where(rows == r, 1.0 - inv_pivot, 0.0))
            else:
                step = col * recip
            schur[b] = schur[b] - col * scaled_row
            inverse[b] = inverse[b] - step * inverse_row
    return jnp.concatenate(inverse, axis=0)


def orthonormal_in_kernel(matrix):
    inner_gram = jnp.dot(matrix.T, matrix, precision=highest_precision,
                         preferred_element_type=jnp.float32)
    lower_inverse = inverse_cholesky(inner_gram)
    return lax.dot_general(
        matrix, lower_inverse, (((1,), (1,)), ((), ())), precision=highest_precision,
        preferred_element_type=jnp.float32,
    )


def orthonormal_kernel(block_ref, basis_ref):
    basis_ref[...] = orthonormal_in_kernel(block_ref[...])


def iterate_kernel(gram_ref, basis_ref, out_ref):
    basis = basis_ref[...]
    for iteration in range(ITERS):
        product = jnp.dot(gram_ref[...], basis, precision=highest_precision,
                          preferred_element_type=jnp.float32)
        basis = orthonormal_in_kernel(product)
    out_ref[...] = basis


def orthonormal(matrix):
    return pl.pallas_call(
        orthonormal_kernel,
        out_shape=jax.ShapeDtypeStruct(matrix.shape, jnp.float32),
    )(matrix)


def subspace_iteration(gram_matrix, mode_basis):
    return pl.pallas_call(
        iterate_kernel,
        out_shape=jax.ShapeDtypeStruct(mode_basis.shape, jnp.float32),
    )(gram_matrix, mode_basis)


def exchange(blocks, axis):
    return lax.all_to_all(blocks, axis, 0, 0, tiled=True)


def reduce_scatter(matrix, axis):
    parts = lax.axis_size(axis)
    blocks = matrix.reshape(parts, matrix.shape[0] // parts, *matrix.shape[1:])
    return exchange(blocks, axis).sum(0)


def gather(matrix, axis):
    parts = lax.axis_size(axis)
    blocks = jnp.broadcast_to(matrix[None], (parts,) + matrix.shape)
    return exchange(blocks, axis).reshape(parts * matrix.shape[0], *matrix.shape[1:])


def pad_rows(matrix, rows):
    return jnp.pad(matrix, ((0, rows - matrix.shape[0]), (0, 0)))


def all_reduce(matrix):
    groups, fibres = lax.axis_size("group"), lax.axis_size("fibre")
    rows = pad_rows(matrix, -(-matrix.shape[0] // groups) * groups)
    rows = reduce_scatter(rows, "group")
    chunk = rows.shape[0]
    rows = pad_rows(rows, -(-chunk // fibres) * fibres)
    rows = reduce_scatter(rows, "fibre")
    rows = gather(rows, "fibre")[:chunk]
    return gather(rows, "group")[:matrix.shape[0]]


def pack_symmetric(gram):
    half = gram.shape[0] // 2
    upper_left, upper_right, lower_right = gram[:half, :half], gram[:half, half:], gram[half:, half:]
    index = jnp.arange(half)
    on_or_above = index[:, None] <= index[None, :]
    triangles = jnp.where(on_or_above, upper_left, lower_right)
    diagonal = jnp.diagonal(lower_right)[None, :]
    return jnp.concatenate([triangles, upper_right, diagonal], axis=0)


def unpack_symmetric(packed):
    half = packed.shape[1]
    triangles, upper_right, diagonal = packed[:half], packed[half:2 * half], packed[2 * half]
    index = jnp.arange(half)
    on_or_above = index[:, None] <= index[None, :]
    below = index[:, None] > index[None, :]
    upper_left = jnp.where(on_or_above, triangles, triangles.T)
    lower_right = jnp.where(below, triangles, triangles.T)
    lower_right = jnp.where(index[:, None] == index[None, :], diagonal[None, :], lower_right)
    return jnp.concatenate([
        jnp.concatenate([upper_left, upper_right], axis=1),
        jnp.concatenate([upper_right.T, lower_right], axis=1),
    ], axis=0)


def on_device(species_field, start_block):
    fibres = lax.all_to_all(species_field, "fibre", split_axis=1, concat_axis=0, tiled=True)
    total_columns = fibres.shape[1] * lax.axis_size("fibre") * lax.axis_size("group")
    fibres, mode_basis = lax.optimization_barrier((fibres, orthonormal(start_block)))
    local_gram = jnp.dot(fibres, fibres.T, precision=highest_precision) / total_columns
    gram_matrix = unpack_symmetric(all_reduce(pack_symmetric(local_gram)))
    mode_basis = subspace_iteration(gram_matrix, mode_basis)
    core_tensor = jnp.dot(mode_basis.T, fibres, precision=highest_precision)
    return (mode_basis, core_tensor)


def solution(mesh):
    placed = (P("fibre", "group"), P())
    return jax.shard_map(
        on_device,
        mesh=mesh,
        in_specs=placed,
        out_specs=(P(), P(None, ("group", "fibre"))),
        check_vma=False,
    )
```

```python
import jax
import jax.numpy as jnp
from jax import lax
from jax.experimental import pallas as pl
from jax.sharding import PartitionSpec as P

ITERS = 3


highest_precision = lax.Precision.HIGHEST
product_precision = lax.Precision.HIGH


def inverse_cholesky(inner_gram):
    size = inner_gram.shape[0]
    count = size // 8
    schur = [inner_gram[8 * b:8 * b + 8, :] for b in range(count)]
    rows = lax.broadcasted_iota(jnp.int32, (8, 1), 0)
    cols = lax.broadcasted_iota(jnp.int32, (1, size), 1)
    inverse = [((rows + 8 * b) == cols).astype(jnp.float32) for b in range(count)]
    for j in range(size):
        pivot_block, r = divmod(j, 8)
        pivot_row = schur[pivot_block][r:r + 1, :]
        inv_pivot = lax.rsqrt(pivot_row[:, j:j + 1])
        recip = inv_pivot * inv_pivot
        scaled_row = jnp.where(cols >= j, pivot_row, 0.0) * recip
        inverse_row = inverse[pivot_block][r:r + 1, :]
        for b in range(pivot_block, count):
            col = schur[b][:, j:j + 1]
            if b == pivot_block:
                col = jnp.where(rows >= r, col, 0.0)
                step = jnp.where(rows > r, col * recip, jnp.where(rows == r, 1.0 - inv_pivot, 0.0))
            else:
                step = col * recip
            schur[b] = schur[b] - col * scaled_row
            inverse[b] = inverse[b] - step * inverse_row
    return jnp.concatenate(inverse, axis=0)


def orthonormal_in_kernel(matrix):
    inner_gram = jnp.dot(matrix.T, matrix, precision=highest_precision,
                         preferred_element_type=jnp.float32)
    lower_inverse = inverse_cholesky(inner_gram)
    return lax.dot_general(
        matrix, lower_inverse, (((1,), (1,)), ((), ())), precision=highest_precision,
        preferred_element_type=jnp.float32,
    )


def orthonormal_kernel(block_ref, basis_ref):
    basis_ref[...] = orthonormal_in_kernel(block_ref[...])


def iterate_kernel(gram_ref, basis_ref, out_ref):
    basis = basis_ref[...]
    for iteration in range(ITERS):
        product = jnp.dot(gram_ref[...], basis, precision=product_precision,
                          preferred_element_type=jnp.float32)
        basis = orthonormal_in_kernel(product)
    out_ref[...] = basis


def orthonormal(matrix):
    return pl.pallas_call(
        orthonormal_kernel,
        out_shape=jax.ShapeDtypeStruct(matrix.shape, jnp.float32),
    )(matrix)


def subspace_iteration(gram_matrix, mode_basis):
    return pl.pallas_call(
        iterate_kernel,
        out_shape=jax.ShapeDtypeStruct(mode_basis.shape, jnp.float32),
    )(gram_matrix, mode_basis)


def exchange(blocks, axis):
    return lax.all_to_all(blocks, axis, 0, 0, tiled=True)


def reduce_scatter(matrix, axis):
    parts = lax.axis_size(axis)
    blocks = matrix.reshape(parts, matrix.shape[0] // parts, *matrix.shape[1:])
    return exchange(blocks, axis).sum(0)


def gather(matrix, axis):
    parts = lax.axis_size(axis)
    blocks = jnp.broadcast_to(matrix[None], (parts,) + matrix.shape)
    return exchange(blocks, axis).reshape(parts * matrix.shape[0], *matrix.shape[1:])


def pad_rows(matrix, rows):
    return jnp.pad(matrix, ((0, rows - matrix.shape[0]), (0, 0)))


def all_reduce(matrix):
    groups, fibres = lax.axis_size("group"), lax.axis_size("fibre")
    rows = pad_rows(matrix, -(-matrix.shape[0] // groups) * groups)
    rows = reduce_scatter(rows, "group")
    chunk = rows.shape[0]
    rows = pad_rows(rows, -(-chunk // fibres) * fibres)
    rows = reduce_scatter(rows, "fibre")
    rows = gather(rows, "fibre")[:chunk]
    return gather(rows, "group")[:matrix.shape[0]]


def pack_symmetric(gram):
    half = gram.shape[0] // 2
    upper_left, upper_right, lower_right = gram[:half, :half], gram[:half, half:], gram[half:, half:]
    index = jnp.arange(half)
    on_or_above = index[:, None] <= index[None, :]
    triangles = jnp.where(on_or_above, upper_left, lower_right)
    diagonal = jnp.diagonal(lower_right)[None, :]
    return jnp.concatenate([triangles, upper_right, diagonal], axis=0)


def unpack_symmetric(packed):
    half = packed.shape[1]
    triangles, upper_right, diagonal = packed[:half], packed[half:2 * half], packed[2 * half]
    index = jnp.arange(half)
    on_or_above = index[:, None] <= index[None, :]
    below = index[:, None] > index[None, :]
    upper_left = jnp.where(on_or_above, triangles, triangles.T)
    lower_right = jnp.where(below, triangles, triangles.T)
    lower_right = jnp.where(index[:, None] == index[None, :], diagonal[None, :], lower_right)
    return jnp.concatenate([
        jnp.concatenate([upper_left, upper_right], axis=1),
        jnp.concatenate([upper_right.T, lower_right], axis=1),
    ], axis=0)


def on_device(species_field, start_block):
    fibres = lax.all_to_all(species_field, "fibre", split_axis=1, concat_axis=0, tiled=True)
    total_columns = fibres.shape[1] * lax.axis_size("fibre") * lax.axis_size("group")
    fibres, mode_basis = lax.optimization_barrier((fibres, orthonormal(start_block)))
    local_gram = jnp.dot(fibres, fibres.T, precision=product_precision) / total_columns
    gram_matrix = unpack_symmetric(all_reduce(pack_symmetric(local_gram)))
    mode_basis = subspace_iteration(gram_matrix, mode_basis)
    core_tensor = jnp.dot(mode_basis.T, fibres, precision=product_precision)
    return (mode_basis, core_tensor)


def solution(mesh):
    placed = (P("fibre", "group"), P())
    return jax.shard_map(
        on_device,
        mesh=mesh,
        in_specs=placed,
        out_specs=(P(), P(None, ("group", "fibre"))),
        check_vma=False,
    )
```

```python
import jax
import jax.numpy as jnp
from jax import lax
from jax.experimental import pallas as pl
from jax.sharding import PartitionSpec as P

ITERS = 3


highest_precision = lax.Precision.HIGHEST
product_precision = lax.Precision.HIGH


def inverse_cholesky(inner_gram):
    size = inner_gram.shape[0]
    count = size // 8
    schur = [inner_gram[8 * b:8 * b + 8, :] for b in range(count)]
    rows = lax.broadcasted_iota(jnp.int32, (8, 1), 0)
    cols = lax.broadcasted_iota(jnp.int32, (1, size), 1)
    inverse = [((rows + 8 * b) == cols).astype(jnp.float32) for b in range(count)]
    for j in range(size):
        pivot_block, r = divmod(j, 8)
        pivot_row = schur[pivot_block][r:r + 1, :]
        inv_pivot = lax.rsqrt(pivot_row[:, j:j + 1])
        recip = inv_pivot * inv_pivot
        scaled_row = jnp.where(cols >= j, pivot_row, 0.0) * recip
        inverse_row = inverse[pivot_block][r:r + 1, :]
        for b in range(pivot_block, count):
            col = schur[b][:, j:j + 1]
            if b == pivot_block:
                col = jnp.where(rows >= r, col, 0.0)
                step = jnp.where(rows > r, col * recip, jnp.where(rows == r, 1.0 - inv_pivot, 0.0))
            else:
                step = col * recip
            schur[b] = schur[b] - col * scaled_row
            inverse[b] = inverse[b] - step * inverse_row
    return jnp.concatenate(inverse, axis=0)


def orthonormal_in_kernel(matrix):
    inner_gram = jnp.dot(matrix.T, matrix, precision=highest_precision,
                         preferred_element_type=jnp.float32)
    lower_inverse = inverse_cholesky(inner_gram)
    return lax.dot_general(
        matrix, lower_inverse, (((1,), (1,)), ((), ())), precision=highest_precision,
        preferred_element_type=jnp.float32,
    )


def orthonormal_kernel(block_ref, basis_ref):
    basis_ref[...] = orthonormal_in_kernel(block_ref[...])


def split_bf16(matrix):
    high = lax.reduce_precision(matrix, exponent_bits=8, mantissa_bits=7)
    return high.astype(jnp.bfloat16), (matrix - high).astype(jnp.bfloat16)


def three_pass_dot(left_high, left_low, right):
    right_high, right_low = split_bf16(right)
    product = jnp.dot(left_high, right_high, preferred_element_type=jnp.float32)
    product += jnp.dot(left_high, right_low, preferred_element_type=jnp.float32)
    product += jnp.dot(left_low, right_high, preferred_element_type=jnp.float32)
    return product


def iterate_kernel(gram_high_ref, gram_low_ref, basis_ref, out_ref):
    basis = basis_ref[...]
    for iteration in range(ITERS):
        product = three_pass_dot(gram_high_ref[...], gram_low_ref[...], basis)
        basis = orthonormal_in_kernel(product)
    out_ref[...] = basis


def orthonormal(matrix):
    return pl.pallas_call(
        orthonormal_kernel,
        out_shape=jax.ShapeDtypeStruct(matrix.shape, jnp.float32),
    )(matrix)


def subspace_iteration(gram_matrix, mode_basis):
    gram_high, gram_low = split_bf16(gram_matrix)
    return pl.pallas_call(
        iterate_kernel,
        out_shape=jax.ShapeDtypeStruct(mode_basis.shape, jnp.float32),
    )(gram_high, gram_low, mode_basis)


def exchange(blocks, axis):
    return lax.all_to_all(blocks, axis, 0, 0, tiled=True)


def reduce_scatter(matrix, axis):
    parts = lax.axis_size(axis)
    blocks = matrix.reshape(parts, matrix.shape[0] // parts, *matrix.shape[1:])
    return exchange(blocks, axis).sum(0)


def gather(matrix, axis):
    parts = lax.axis_size(axis)
    blocks = jnp.broadcast_to(matrix[None], (parts,) + matrix.shape)
    return exchange(blocks, axis).reshape(parts * matrix.shape[0], *matrix.shape[1:])


def pad_rows(matrix, rows):
    return jnp.pad(matrix, ((0, rows - matrix.shape[0]), (0, 0)))


def all_reduce(matrix):
    groups, fibres = lax.axis_size("group"), lax.axis_size("fibre")
    rows = pad_rows(matrix, -(-matrix.shape[0] // groups) * groups)
    rows = reduce_scatter(rows, "group")
    chunk = rows.shape[0]
    rows = pad_rows(rows, -(-chunk // fibres) * fibres)
    rows = reduce_scatter(rows, "fibre")
    rows = gather(rows, "fibre")[:chunk]
    return gather(rows, "group")[:matrix.shape[0]]


def pack_symmetric(gram):
    half = gram.shape[0] // 2
    upper_left, upper_right, lower_right = gram[:half, :half], gram[:half, half:], gram[half:, half:]
    index = jnp.arange(half)
    on_or_above = index[:, None] <= index[None, :]
    triangles = jnp.where(on_or_above, upper_left, lower_right)
    diagonal = jnp.diagonal(lower_right)[None, :]
    return jnp.concatenate([triangles, upper_right, diagonal], axis=0)


def unpack_symmetric(packed):
    half = packed.shape[1]
    triangles, upper_right, diagonal = packed[:half], packed[half:2 * half], packed[2 * half]
    index = jnp.arange(half)
    on_or_above = index[:, None] <= index[None, :]
    below = index[:, None] > index[None, :]
    upper_left = jnp.where(on_or_above, triangles, triangles.T)
    lower_right = jnp.where(below, triangles, triangles.T)
    lower_right = jnp.where(index[:, None] == index[None, :], diagonal[None, :], lower_right)
    return jnp.concatenate([
        jnp.concatenate([upper_left, upper_right], axis=1),
        jnp.concatenate([upper_right.T, lower_right], axis=1),
    ], axis=0)


def on_device(species_field, start_block):
    fibres = lax.all_to_all(species_field, "fibre", split_axis=1, concat_axis=0, tiled=True)
    total_columns = fibres.shape[1] * lax.axis_size("fibre") * lax.axis_size("group")
    fibres, mode_basis = lax.optimization_barrier((fibres, orthonormal(start_block)))
    local_gram = jnp.dot(fibres, fibres.T, precision=product_precision) / total_columns
    gram_matrix = unpack_symmetric(all_reduce(pack_symmetric(local_gram)))
    mode_basis = subspace_iteration(gram_matrix, mode_basis)
    core_tensor = jnp.dot(mode_basis.T, fibres, precision=product_precision)
    return (mode_basis, core_tensor)


def solution(mesh):
    placed = (P("fibre", "group"), P())
    return jax.shard_map(
        on_device,
        mesh=mesh,
        in_specs=placed,
        out_specs=(P(), P(None, ("group", "fibre"))),
        check_vma=False,
    )
```

```python
import jax
import jax.numpy as jnp
from jax import lax
from jax.experimental import pallas as pl
from jax.experimental.pallas import tpu as pltpu
from jax.sharding import PartitionSpec as P

ITERS = 3


highest_precision = lax.Precision.HIGHEST
product_precision = lax.Precision.HIGH


def inverse_cholesky(inner_gram):
    size = inner_gram.shape[0]
    count = size // 8
    schur = [inner_gram[8 * b:8 * b + 8, :] for b in range(count)]
    rows = lax.broadcasted_iota(jnp.int32, (8, 1), 0)
    cols = lax.broadcasted_iota(jnp.int32, (1, size), 1)
    inverse = [((rows + 8 * b) == cols).astype(jnp.float32) for b in range(count)]
    for j in range(size):
        pivot_block, r = divmod(j, 8)
        pivot_row = schur[pivot_block][r:r + 1, :]
        inv_pivot = lax.rsqrt(pivot_row[:, j:j + 1])
        recip = inv_pivot * inv_pivot
        scaled_row = jnp.where(cols >= j, pivot_row, 0.0) * recip
        inverse_row = inverse[pivot_block][r:r + 1, :]
        for b in range(pivot_block, count):
            col = schur[b][:, j:j + 1]
            if b == pivot_block:
                col = jnp.where(rows >= r, col, 0.0)
                step = jnp.where(rows > r, col * recip, jnp.where(rows == r, 1.0 - inv_pivot, 0.0))
            else:
                step = col * recip
            schur[b] = schur[b] - col * scaled_row
            inverse[b] = inverse[b] - step * inverse_row
    return jnp.concatenate(inverse, axis=0)


def orthonormal_in_kernel(matrix):
    inner_gram = jnp.dot(matrix.T, matrix, precision=highest_precision,
                         preferred_element_type=jnp.float32)
    lower_inverse = inverse_cholesky(inner_gram)
    return lax.dot_general(
        matrix, lower_inverse, (((1,), (1,)), ((), ())), precision=highest_precision,
        preferred_element_type=jnp.float32,
    )


def orthonormal_kernel(block_ref, basis_ref):
    basis_ref[...] = orthonormal_in_kernel(block_ref[...])


def iterate_kernel(packed_ref, basis_ref, out_ref, gram_ref):
    half = packed_ref.shape[1]
    triangles = packed_ref[0:half, :]
    upper_right = packed_ref[half:2 * half, :]
    diagonal = packed_ref[2 * half:2 * half + 1, :]
    rows = lax.broadcasted_iota(jnp.int32, (half, 1), 0)
    cols = lax.broadcasted_iota(jnp.int32, (1, half), 1)
    mirrored = triangles.T
    gram_ref[0:half, 0:half] = jnp.where(rows <= cols, triangles, mirrored)
    lower_right = jnp.where(rows > cols, triangles, mirrored)
    gram_ref[half:, half:] = jnp.where(rows == cols, diagonal, lower_right)
    gram_ref[0:half, half:] = upper_right
    gram_ref[half:, 0:half] = upper_right.T
    basis = basis_ref[...]
    for iteration in range(ITERS):
        product = jnp.dot(gram_ref[...], basis, precision=product_precision,
                          preferred_element_type=jnp.float32)
        basis = orthonormal_in_kernel(product)
    out_ref[...] = basis


def orthonormal(matrix):
    return pl.pallas_call(
        orthonormal_kernel,
        out_shape=jax.ShapeDtypeStruct(matrix.shape, jnp.float32),
    )(matrix)


def subspace_iteration(packed_gram, mode_basis):
    size = 2 * packed_gram.shape[1]
    return pl.pallas_call(
        iterate_kernel,
        out_shape=jax.ShapeDtypeStruct(mode_basis.shape, jnp.float32),
        scratch_shapes=[pltpu.VMEM((size, size), jnp.float32)],
    )(packed_gram, mode_basis)


def exchange(blocks, axis):
    return lax.all_to_all(blocks, axis, 0, 0, tiled=True)


def reduce_scatter(matrix, axis):
    parts = lax.axis_size(axis)
    blocks = matrix.reshape(parts, matrix.shape[0] // parts, *matrix.shape[1:])
    return exchange(blocks, axis).sum(0)


def gather(matrix, axis):
    parts = lax.axis_size(axis)
    blocks = jnp.broadcast_to(matrix[None], (parts,) + matrix.shape)
    return exchange(blocks, axis).reshape(parts * matrix.shape[0], *matrix.shape[1:])


def pad_rows(matrix, rows):
    return jnp.pad(matrix, ((0, rows - matrix.shape[0]), (0, 0)))


def all_reduce(matrix):
    groups, fibres = lax.axis_size("group"), lax.axis_size("fibre")
    rows = pad_rows(matrix, -(-matrix.shape[0] // groups) * groups)
    rows = reduce_scatter(rows, "group")
    chunk = rows.shape[0]
    rows = pad_rows(rows, -(-chunk // fibres) * fibres)
    rows = reduce_scatter(rows, "fibre")
    rows = gather(rows, "fibre")[:chunk]
    return gather(rows, "group")


def pack_symmetric(gram):
    half = gram.shape[0] // 2
    upper_left, upper_right, lower_right = gram[:half, :half], gram[:half, half:], gram[half:, half:]
    index = jnp.arange(half)
    on_or_above = index[:, None] <= index[None, :]
    triangles = jnp.where(on_or_above, upper_left, lower_right)
    diagonal = jnp.diagonal(lower_right)[None, :]
    return jnp.concatenate([triangles, upper_right, diagonal], axis=0)


def on_device(species_field, start_block):
    fibres = lax.all_to_all(species_field, "fibre", split_axis=1, concat_axis=0, tiled=True)
    total_columns = fibres.shape[1] * lax.axis_size("fibre") * lax.axis_size("group")
    fibres, mode_basis = lax.optimization_barrier((fibres, orthonormal(start_block)))
    local_gram = jnp.dot(fibres, fibres.T, precision=product_precision) / total_columns
    packed_gram = all_reduce(pack_symmetric(local_gram))
    mode_basis = subspace_iteration(packed_gram, mode_basis)
    core_tensor = jnp.dot(mode_basis.T, fibres, precision=product_precision)
    return (mode_basis, core_tensor)


def solution(mesh):
    placed = (P("fibre", "group"), P())
    return jax.shard_map(
        on_device,
        mesh=mesh,
        in_specs=placed,
        out_specs=(P(), P(None, ("group", "fibre"))),
        check_vma=False,
    )
```

```python
import jax
import jax.numpy as jnp
from jax import lax
from jax.experimental import pallas as pl
from jax.experimental.pallas import tpu as pltpu
from jax.sharding import PartitionSpec as P

ITERS = 3


highest_precision = lax.Precision.HIGHEST
product_precision = lax.Precision.HIGH


def inverse_cholesky(inner_gram):
    size = inner_gram.shape[0]
    count = size // 8
    schur = [inner_gram[8 * b:8 * b + 8, :] for b in range(count)]
    rows = lax.broadcasted_iota(jnp.int32, (8, 1), 0)
    cols = lax.broadcasted_iota(jnp.int32, (1, size), 1)
    inverse = [((rows + 8 * b) == cols).astype(jnp.float32) for b in range(count)]
    for j in range(size):
        pivot_block, r = divmod(j, 8)
        pivot_row = schur[pivot_block][r:r + 1, :]
        inv_pivot = lax.rsqrt(pivot_row[:, j:j + 1])
        recip = inv_pivot * inv_pivot
        scaled_row = jnp.where(cols >= j, pivot_row, 0.0) * recip
        inverse_row = inverse[pivot_block][r:r + 1, :]
        for b in range(pivot_block, count):
            col = schur[b][:, j:j + 1]
            if b == pivot_block:
                col = jnp.where(rows >= r, col, 0.0)
                step = jnp.where(rows > r, col * recip, jnp.where(rows == r, 1.0 - inv_pivot, 0.0))
            else:
                step = col * recip
            schur[b] = schur[b] - col * scaled_row
            inverse[b] = inverse[b] - step * inverse_row
    return jnp.concatenate(inverse, axis=0)


def orthonormal_in_kernel(matrix):
    inner_gram = jnp.dot(matrix.T, matrix, precision=highest_precision,
                         preferred_element_type=jnp.float32)
    lower_inverse = inverse_cholesky(inner_gram)
    return lax.dot_general(
        matrix, lower_inverse, (((1,), (1,)), ((), ())), precision=highest_precision,
        preferred_element_type=jnp.float32,
    )


def orthonormal_kernel(block_ref, basis_ref):
    basis_ref[...] = orthonormal_in_kernel(block_ref[...])


def iterate_kernel(packed_ref, basis_ref, out_ref, gram_ref):
    half = packed_ref.shape[1]
    triangles = packed_ref[0:half, :]
    upper_right = packed_ref[half:2 * half, :]
    diagonal = packed_ref[2 * half:2 * half + 1, :]
    rows = lax.broadcasted_iota(jnp.int32, (half, 1), 0)
    cols = lax.broadcasted_iota(jnp.int32, (1, half), 1)
    mirrored = triangles.T
    gram_ref[0:half, 0:half] = jnp.where(rows <= cols, triangles, mirrored)
    lower_right = jnp.where(rows > cols, triangles, mirrored)
    gram_ref[half:, half:] = jnp.where(rows == cols, diagonal, lower_right)
    gram_ref[0:half, half:] = upper_right
    gram_ref[half:, 0:half] = upper_right.T
    basis = basis_ref[...]
    for iteration in range(ITERS):
        product = jnp.dot(gram_ref[...], basis, precision=product_precision,
                          preferred_element_type=jnp.float32)
        basis = orthonormal_in_kernel(product)
    out_ref[...] = basis


def orthonormal(matrix):
    return pl.pallas_call(
        orthonormal_kernel,
        out_shape=jax.ShapeDtypeStruct(matrix.shape, jnp.float32),
    )(matrix)


def subspace_iteration(packed_gram, mode_basis):
    size = 2 * packed_gram.shape[1]
    return pl.pallas_call(
        iterate_kernel,
        out_shape=jax.ShapeDtypeStruct(mode_basis.shape, jnp.float32),
        scratch_shapes=[pltpu.VMEM((size, size), jnp.float32)],
    )(packed_gram, mode_basis)


def exchange(blocks, axis):
    return lax.all_to_all(blocks, axis, 0, 0, tiled=True)


def reduce_scatter(matrix, axis):
    parts = lax.axis_size(axis)
    blocks = matrix.reshape(parts, matrix.shape[0] // parts, *matrix.shape[1:])
    return exchange(blocks, axis).sum(0)


def gather(matrix, axis):
    parts = lax.axis_size(axis)
    blocks = jnp.broadcast_to(matrix[None], (parts,) + matrix.shape)
    return exchange(blocks, axis).reshape(parts * matrix.shape[0], *matrix.shape[1:])


def pad_rows(matrix, rows):
    return jnp.pad(matrix, ((0, rows - matrix.shape[0]), (0, 0)))


def all_reduce(matrix):
    groups, fibres = lax.axis_size("group"), lax.axis_size("fibre")
    rows = pad_rows(matrix, -(-matrix.shape[0] // groups) * groups)
    rows = reduce_scatter(rows, "group")
    chunk = rows.shape[0]
    rows = pad_rows(rows, -(-chunk // fibres) * fibres)
    rows = reduce_scatter(rows, "fibre")
    rows = gather(rows, "fibre")[:chunk]
    return gather(rows, "group")


def pack_symmetric(gram):
    half = gram.shape[0] // 2
    upper_left, upper_right, lower_right = gram[:half, :half], gram[:half, half:], gram[half:, half:]
    index = jnp.arange(half)
    on_or_above = index[:, None] <= index[None, :]
    triangles = jnp.where(on_or_above, upper_left, lower_right)
    diagonal = jnp.diagonal(lower_right)[None, :]
    return jnp.concatenate([triangles, upper_right, diagonal], axis=0)


def chunk_copy_kernel(field_ref, chunks_ref, semaphores):
    parts, width = chunks_ref.shape[0], chunks_ref.shape[2]
    copies = [
        pltpu.make_async_copy(field_ref.at[:, part * width:(part + 1) * width],
                              chunks_ref.at[part], semaphores.at[part])
        for part in range(parts)
    ]
    for copy in copies:
        copy.start()
    for copy in copies:
        copy.wait()


def column_chunks(field, parts):
    rows, columns = field.shape
    return pl.pallas_call(
        chunk_copy_kernel,
        out_shape=jax.ShapeDtypeStruct((parts, rows, columns // parts), field.dtype),
        in_specs=[pl.BlockSpec(memory_space=pl.ANY)],
        out_specs=pl.BlockSpec(memory_space=pl.ANY),
        scratch_shapes=[pltpu.SemaphoreType.DMA((parts,))],
    )(field)


def on_device(species_field, start_block):
    parts = lax.axis_size("fibre")
    chunks = column_chunks(species_field, parts)
    fibres = lax.all_to_all(chunks, "fibre", 0, 0, tiled=True)
    fibres = fibres.reshape(parts * species_field.shape[0], -1)
    total_columns = fibres.shape[1] * lax.axis_size("fibre") * lax.axis_size("group")
    fibres, mode_basis = lax.optimization_barrier((fibres, orthonormal(start_block)))
    local_gram = jnp.dot(fibres, fibres.T, precision=product_precision) / total_columns
    packed_gram = all_reduce(pack_symmetric(local_gram))
    mode_basis = subspace_iteration(packed_gram, mode_basis)
    core_tensor = jnp.dot(mode_basis.T, fibres, precision=product_precision)
    return (mode_basis, core_tensor)


def solution(mesh):
    placed = (P("fibre", "group"), P())
    return jax.shard_map(
        on_device,
        mesh=mesh,
        in_specs=placed,
        out_specs=(P(), P(None, ("group", "fibre"))),
        check_vma=False,
    )
```

```python
import jax
import jax.numpy as jnp
from jax import lax
from jax.experimental import pallas as pl
from jax.experimental.pallas import tpu as pltpu
from jax.sharding import PartitionSpec as P

ITERS = 3


highest_precision = lax.Precision.HIGHEST
product_precision = lax.Precision.HIGH


def inverse_cholesky(inner_gram):
    size = inner_gram.shape[0]
    count = size // 8
    schur = [inner_gram[8 * b:8 * b + 8, :] for b in range(count)]
    rows = lax.broadcasted_iota(jnp.int32, (8, 1), 0)
    cols = lax.broadcasted_iota(jnp.int32, (1, size), 1)
    inverse = [((rows + 8 * b) == cols).astype(jnp.float32) for b in range(count)]
    for j in range(size):
        pivot_block, r = divmod(j, 8)
        pivot_row = schur[pivot_block][r:r + 1, :]
        inv_pivot = lax.rsqrt(pivot_row[:, j:j + 1])
        recip = inv_pivot * inv_pivot
        scaled_row = jnp.where(cols >= j, pivot_row, 0.0) * recip
        inverse_row = inverse[pivot_block][r:r + 1, :]
        for b in range(pivot_block, count):
            col = schur[b][:, j:j + 1]
            if b == pivot_block:
                col = jnp.where(rows >= r, col, 0.0)
                step = jnp.where(rows > r, col * recip, jnp.where(rows == r, 1.0 - inv_pivot, 0.0))
            else:
                step = col * recip
            schur[b] = schur[b] - col * scaled_row
            inverse[b] = inverse[b] - step * inverse_row
    return jnp.concatenate(inverse, axis=0)


def orthonormal_in_kernel(matrix):
    inner_gram = jnp.dot(matrix.T, matrix, precision=highest_precision,
                         preferred_element_type=jnp.float32)
    lower_inverse = inverse_cholesky(inner_gram)
    return lax.dot_general(
        matrix, lower_inverse, (((1,), (1,)), ((), ())), precision=highest_precision,
        preferred_element_type=jnp.float32,
    )


def orthonormal_kernel(block_ref, basis_ref):
    basis_ref[...] = orthonormal_in_kernel(block_ref[...])


def iterate_kernel(packed_ref, basis_ref, out_ref, gram_ref):
    half = packed_ref.shape[1]
    triangles = packed_ref[0:half, :]
    upper_right = packed_ref[half:2 * half, :]
    diagonal = packed_ref[2 * half:2 * half + 1, :]
    rows = lax.broadcasted_iota(jnp.int32, (half, 1), 0)
    cols = lax.broadcasted_iota(jnp.int32, (1, half), 1)
    mirrored = triangles.T
    gram_ref[0:half, 0:half] = jnp.where(rows <= cols, triangles, mirrored)
    lower_right = jnp.where(rows > cols, triangles, mirrored)
    gram_ref[half:, half:] = jnp.where(rows == cols, diagonal, lower_right)
    gram_ref[0:half, half:] = upper_right
    gram_ref[half:, 0:half] = upper_right.T
    basis = basis_ref[...]
    for iteration in range(ITERS):
        product = jnp.dot(gram_ref[...], basis, precision=product_precision,
                          preferred_element_type=jnp.float32)
        basis = orthonormal_in_kernel(product)
    out_ref[...] = basis


def orthonormal(matrix):
    return pl.pallas_call(
        orthonormal_kernel,
        out_shape=jax.ShapeDtypeStruct(matrix.shape, jnp.float32),
    )(matrix)


def subspace_iteration(packed_gram, mode_basis):
    size = 2 * packed_gram.shape[1]
    return pl.pallas_call(
        iterate_kernel,
        out_shape=jax.ShapeDtypeStruct(mode_basis.shape, jnp.float32),
        scratch_shapes=[pltpu.VMEM((size, size), jnp.float32)],
    )(packed_gram, mode_basis)


def exchange(blocks, axis):
    return lax.all_to_all(blocks, axis, 0, 0, tiled=True)


def reduce_scatter(matrix, axis):
    parts = lax.axis_size(axis)
    blocks = matrix.reshape(parts, matrix.shape[0] // parts, *matrix.shape[1:])
    return exchange(blocks, axis).sum(0)


def gather(matrix, axis):
    parts = lax.axis_size(axis)
    blocks = jnp.broadcast_to(matrix[None], (parts,) + matrix.shape)
    return exchange(blocks, axis).reshape(parts * matrix.shape[0], *matrix.shape[1:])


def pad_rows(matrix, rows):
    return jnp.pad(matrix, ((0, rows - matrix.shape[0]), (0, 0)))


def all_reduce(matrix):
    groups, fibres = lax.axis_size("group"), lax.axis_size("fibre")
    rows = pad_rows(matrix, -(-matrix.shape[0] // groups) * groups)
    rows = reduce_scatter(rows, "group")
    chunk = rows.shape[0]
    rows = pad_rows(rows, -(-chunk // fibres) * fibres)
    rows = reduce_scatter(rows, "fibre")
    rows = gather(rows, "fibre")[:chunk]
    return gather(rows, "group")


def pack_symmetric(gram):
    half = gram.shape[0] // 2
    upper_left, upper_right, lower_right = gram[:half, :half], gram[:half, half:], gram[half:, half:]
    index = jnp.arange(half)
    on_or_above = index[:, None] <= index[None, :]
    triangles = jnp.where(on_or_above, upper_left, lower_right)
    on_diagonal = index[:, None] == index[None, :]
    diagonal = jnp.sum(jnp.where(on_diagonal, lower_right, 0.0), axis=0, keepdims=True)
    return jnp.concatenate([triangles, upper_right, diagonal], axis=0)


def on_device(species_field, start_block):
    fibres = lax.all_to_all(species_field, "fibre", split_axis=1, concat_axis=0, tiled=True)
    total_columns = fibres.shape[1] * lax.axis_size("fibre") * lax.axis_size("group")
    fibres, mode_basis = lax.optimization_barrier((fibres, orthonormal(start_block)))
    local_gram = jnp.dot(fibres, fibres.T, precision=product_precision) / total_columns
    packed_gram = all_reduce(pack_symmetric(local_gram))
    mode_basis = subspace_iteration(packed_gram, mode_basis)
    core_tensor = jnp.dot(mode_basis.T, fibres, precision=product_precision)
    return (mode_basis, core_tensor)


def solution(mesh):
    placed = (P("fibre", "group"), P())
    return jax.shard_map(
        on_device,
        mesh=mesh,
        in_specs=placed,
        out_specs=(P(), P(None, ("group", "fibre"))),
        check_vma=False,
    )
```

```python
import jax
import jax.numpy as jnp
from jax import lax
from jax.experimental import pallas as pl
from jax.experimental.pallas import tpu as pltpu
from jax.sharding import PartitionSpec as P

ITERS = 3


highest_precision = lax.Precision.HIGHEST
product_precision = lax.Precision.HIGH


def inverse_cholesky(inner_gram):
    size = inner_gram.shape[0]
    count = size // 8
    schur = [inner_gram[8 * b:8 * b + 8, :] for b in range(count)]
    rows = lax.broadcasted_iota(jnp.int32, (8, 1), 0)
    cols = lax.broadcasted_iota(jnp.int32, (1, size), 1)
    inverse = [((rows + 8 * b) == cols).astype(jnp.float32) for b in range(count)]
    for j in range(size):
        pivot_block, r = divmod(j, 8)
        pivot_row = schur[pivot_block][r:r + 1, :]
        inv_pivot = lax.rsqrt(pivot_row[:, j:j + 1])
        recip = inv_pivot * inv_pivot
        scaled_row = jnp.where(cols >= j, pivot_row, 0.0) * recip
        inverse_row = inverse[pivot_block][r:r + 1, :]
        for b in range(pivot_block, count):
            col = schur[b][:, j:j + 1]
            if b == pivot_block:
                col = jnp.where(rows >= r, col, 0.0)
                step = jnp.where(rows > r, col * recip, jnp.where(rows == r, 1.0 - inv_pivot, 0.0))
            else:
                step = col * recip
            schur[b] = schur[b] - col * scaled_row
            inverse[b] = inverse[b] - step * inverse_row
    return jnp.concatenate(inverse, axis=0)


def orthonormal_in_kernel(matrix):
    inner_gram = jnp.dot(matrix.T, matrix, precision=highest_precision,
                         preferred_element_type=jnp.float32)
    lower_inverse = inverse_cholesky(inner_gram)
    return lax.dot_general(
        matrix, lower_inverse, (((1,), (1,)), ((), ())), precision=highest_precision,
        preferred_element_type=jnp.float32,
    )


def orthonormal_kernel(block_ref, basis_ref):
    basis_ref[...] = orthonormal_in_kernel(block_ref[...])


def iterate_kernel(packed_ref, basis_ref, out_ref, gram_ref):
    half = packed_ref.shape[1]
    triangles = packed_ref[0:half, :]
    upper_right = packed_ref[half:2 * half, :]
    diagonal = packed_ref[2 * half:2 * half + 1, :]
    rows = lax.broadcasted_iota(jnp.int32, (half, 1), 0)
    cols = lax.broadcasted_iota(jnp.int32, (1, half), 1)
    mirrored = triangles.T
    gram_ref[0:half, 0:half] = jnp.where(rows <= cols, triangles, mirrored)
    lower_right = jnp.where(rows > cols, triangles, mirrored)
    gram_ref[half:, half:] = jnp.where(rows == cols, diagonal, lower_right)
    gram_ref[0:half, half:] = upper_right
    gram_ref[half:, 0:half] = upper_right.T
    basis = basis_ref[...]
    for iteration in range(ITERS - 1):
        product = jnp.dot(gram_ref[...], basis, precision=product_precision,
                          preferred_element_type=jnp.float32)
        basis = orthonormal_in_kernel(product)
    product = jnp.dot(gram_ref[...], basis, precision=product_precision,
                      preferred_element_type=jnp.float32)
    inner_gram = jnp.dot(product.T, product, precision=highest_precision,
                         preferred_element_type=jnp.float32)
    out_ref[...] = lax.dot_general(
        inverse_cholesky(inner_gram), product, (((1,), (1,)), ((), ())),
        precision=highest_precision, preferred_element_type=jnp.float32,
    )


def orthonormal(matrix):
    return pl.pallas_call(
        orthonormal_kernel,
        out_shape=jax.ShapeDtypeStruct(matrix.shape, jnp.float32),
    )(matrix)


def subspace_iteration(packed_gram, mode_basis):
    size = 2 * packed_gram.shape[1]
    return pl.pallas_call(
        iterate_kernel,
        out_shape=jax.ShapeDtypeStruct(mode_basis.shape[::-1], jnp.float32),
        scratch_shapes=[pltpu.VMEM((size, size), jnp.float32)],
    )(packed_gram, mode_basis)


def exchange(blocks, axis):
    return lax.all_to_all(blocks, axis, 0, 0, tiled=True)


def reduce_scatter(matrix, axis):
    parts = lax.axis_size(axis)
    blocks = matrix.reshape(parts, matrix.shape[0] // parts, *matrix.shape[1:])
    return exchange(blocks, axis).sum(0)


def gather(matrix, axis):
    parts = lax.axis_size(axis)
    blocks = jnp.broadcast_to(matrix[None], (parts,) + matrix.shape)
    return exchange(blocks, axis).reshape(parts * matrix.shape[0], *matrix.shape[1:])


def pad_rows(matrix, rows):
    return jnp.pad(matrix, ((0, rows - matrix.shape[0]), (0, 0)))


def all_reduce(matrix):
    groups, fibres = lax.axis_size("group"), lax.axis_size("fibre")
    rows = pad_rows(matrix, -(-matrix.shape[0] // groups) * groups)
    rows = reduce_scatter(rows, "group")
    chunk = rows.shape[0]
    rows = pad_rows(rows, -(-chunk // fibres) * fibres)
    rows = reduce_scatter(rows, "fibre")
    rows = gather(rows, "fibre")[:chunk]
    return gather(rows, "group")


def pack_symmetric(gram):
    half = gram.shape[0] // 2
    upper_left, upper_right, lower_right = gram[:half, :half], gram[:half, half:], gram[half:, half:]
    index = jnp.arange(half)
    on_or_above = index[:, None] <= index[None, :]
    triangles = jnp.where(on_or_above, upper_left, lower_right)
    on_diagonal = index[:, None] == index[None, :]
    diagonal = jnp.sum(jnp.where(on_diagonal, lower_right, 0.0), axis=0, keepdims=True)
    return jnp.concatenate([triangles, upper_right, diagonal], axis=0)


def on_device(species_field, start_block):
    fibres = lax.all_to_all(species_field, "fibre", split_axis=1, concat_axis=0, tiled=True)
    total_columns = fibres.shape[1] * lax.axis_size("fibre") * lax.axis_size("group")
    fibres, mode_basis = lax.optimization_barrier((fibres, orthonormal(start_block)))
    local_gram = jnp.dot(fibres, fibres.T, precision=product_precision) / total_columns
    packed_gram = all_reduce(pack_symmetric(local_gram))
    basis_rows = subspace_iteration(packed_gram, mode_basis)
    core_tensor = jnp.dot(basis_rows, fibres, precision=product_precision)
    return (basis_rows.T, core_tensor)


def solution(mesh):
    placed = (P("fibre", "group"), P())
    return jax.shard_map(
        on_device,
        mesh=mesh,
        in_specs=placed,
        out_specs=(P(), P(None, ("group", "fibre"))),
        check_vma=False,
    )
```

```python
import jax
import jax.numpy as jnp
from jax import lax
from jax.experimental import pallas as pl
from jax.experimental.pallas import tpu as pltpu
from jax.sharding import PartitionSpec as P

ITERS = 3


highest_precision = lax.Precision.HIGHEST
product_precision = lax.Precision.HIGH


def inverse_cholesky(inner_gram):
    size = inner_gram.shape[0]
    count = size // 8
    schur = [inner_gram[8 * b:8 * b + 8, :] for b in range(count)]
    rows = lax.broadcasted_iota(jnp.int32, (8, 1), 0)
    cols = lax.broadcasted_iota(jnp.int32, (1, size), 1)
    inverse = [((rows + 8 * b) == cols).astype(jnp.float32) for b in range(count)]
    for j in range(size):
        pivot_block, r = divmod(j, 8)
        pivot_row = schur[pivot_block][r:r + 1, :]
        inv_pivot = lax.rsqrt(pivot_row[:, j:j + 1])
        recip = inv_pivot * inv_pivot
        scaled_row = jnp.where(cols >= j, pivot_row, 0.0) * recip
        inverse_row = inverse[pivot_block][r:r + 1, :]
        for b in range(pivot_block, count):
            col = schur[b][:, j:j + 1]
            if b == pivot_block:
                col = jnp.where(rows >= r, col, 0.0)
                step = jnp.where(rows > r, col * recip, jnp.where(rows == r, 1.0 - inv_pivot, 0.0))
            else:
                step = col * recip
            schur[b] = schur[b] - col * scaled_row
            inverse[b] = inverse[b] - step * inverse_row
    return jnp.concatenate(inverse, axis=0)


def orthonormal_in_kernel(matrix):
    inner_gram = jnp.dot(matrix.T, matrix, precision=highest_precision,
                         preferred_element_type=jnp.float32)
    lower_inverse = inverse_cholesky(inner_gram)
    return lax.dot_general(
        matrix, lower_inverse, (((1,), (1,)), ((), ())), precision=highest_precision,
        preferred_element_type=jnp.float32,
    )


def orthonormal_kernel(block_ref, basis_ref):
    basis_ref[...] = orthonormal_in_kernel(block_ref[...])


def iterate_kernel(packed_ref, basis_ref, out_ref, gram_ref):
    half = packed_ref.shape[1]
    triangles = packed_ref[0:half, :]
    upper_right = packed_ref[half:2 * half, :]
    diagonal = packed_ref[2 * half:2 * half + 1, :]
    rows = lax.broadcasted_iota(jnp.int32, (half, 1), 0)
    cols = lax.broadcasted_iota(jnp.int32, (1, half), 1)
    mirrored = triangles.T
    gram_ref[0:half, 0:half] = jnp.where(rows <= cols, triangles, mirrored)
    lower_right = jnp.where(rows > cols, triangles, mirrored)
    gram_ref[half:, half:] = jnp.where(rows == cols, diagonal, lower_right)
    gram_ref[0:half, half:] = upper_right
    gram_ref[half:, 0:half] = upper_right.T
    basis = basis_ref[...]
    for iteration in range(ITERS - 1):
        product = jnp.dot(gram_ref[...], basis, precision=product_precision,
                          preferred_element_type=jnp.float32)
        basis = orthonormal_in_kernel(product)
    product = jnp.dot(gram_ref[...], basis, precision=product_precision,
                      preferred_element_type=jnp.float32)
    inner_gram = jnp.dot(product.T, product, precision=highest_precision,
                         preferred_element_type=jnp.float32)
    out_ref[...] = lax.dot_general(
        inverse_cholesky(inner_gram), product, (((1,), (1,)), ((), ())),
        precision=highest_precision, preferred_element_type=jnp.float32,
    )


def orthonormal(matrix):
    return pl.pallas_call(
        orthonormal_kernel,
        out_shape=jax.ShapeDtypeStruct(matrix.shape, jnp.float32),
    )(matrix)


def subspace_iteration(packed_gram, mode_basis):
    size = 2 * packed_gram.shape[1]
    return pl.pallas_call(
        iterate_kernel,
        out_shape=jax.ShapeDtypeStruct(mode_basis.shape[::-1], jnp.float32),
        scratch_shapes=[pltpu.VMEM((size, size), jnp.float32)],
    )(packed_gram, mode_basis)


def exchange(blocks, axis):
    return lax.all_to_all(blocks, axis, 0, 0, tiled=True)


def reduce_scatter(matrix, axis):
    parts = lax.axis_size(axis)
    blocks = matrix.reshape(parts, matrix.shape[0] // parts, *matrix.shape[1:])
    return exchange(blocks, axis).sum(0)


def gather(matrix, axis):
    parts = lax.axis_size(axis)
    blocks = jnp.broadcast_to(matrix[None], (parts,) + matrix.shape)
    return exchange(blocks, axis).reshape(parts * matrix.shape[0], *matrix.shape[1:])


def pad_rows(matrix, rows):
    return jnp.pad(matrix, ((0, rows - matrix.shape[0]), (0, 0)))


def all_reduce(matrix):
    groups, fibres = lax.axis_size("group"), lax.axis_size("fibre")
    chunk = -(-matrix.shape[0] // groups)
    rows = pad_rows(matrix, -(-chunk // 8) * 8 * groups)
    rows = reduce_scatter(rows, "group")
    chunk = rows.shape[0]
    rows = pad_rows(rows, -(-chunk // fibres) * fibres)
    rows = reduce_scatter(rows, "fibre")
    rows = gather(rows, "fibre")[:chunk]
    return gather(rows, "group")


def pack_symmetric(gram):
    half = gram.shape[0] // 2
    upper_left, upper_right, lower_right = gram[:half, :half], gram[:half, half:], gram[half:, half:]
    index = jnp.arange(half)
    on_or_above = index[:, None] <= index[None, :]
    triangles = jnp.where(on_or_above, upper_left, lower_right)
    on_diagonal = index[:, None] == index[None, :]
    diagonal = jnp.sum(jnp.where(on_diagonal, lower_right, 0.0), axis=0, keepdims=True)
    return jnp.concatenate([triangles, upper_right, diagonal], axis=0)


def on_device(species_field, start_block):
    fibres = lax.all_to_all(species_field, "fibre", split_axis=1, concat_axis=0, tiled=True)
    total_columns = fibres.shape[1] * lax.axis_size("fibre") * lax.axis_size("group")
    fibres, mode_basis = lax.optimization_barrier((fibres, orthonormal(start_block)))
    local_gram = jnp.dot(fibres, fibres.T, precision=product_precision) / total_columns
    packed_gram = all_reduce(pack_symmetric(local_gram))
    basis_rows = subspace_iteration(packed_gram, mode_basis)
    core_tensor = jnp.dot(basis_rows, fibres, precision=product_precision)
    return (basis_rows.T, core_tensor)


def solution(mesh):
    placed = (P("fibre", "group"), P())
    return jax.shard_map(
        on_device,
        mesh=mesh,
        in_specs=placed,
        out_specs=(P(), P(None, ("group", "fibre"))),
        check_vma=False,
    )
```

```python
import jax
import jax.numpy as jnp
from jax import lax
from jax.experimental import pallas as pl
from jax.experimental.pallas import tpu as pltpu
from jax.sharding import PartitionSpec as P

ITERS = 3


highest_precision = lax.Precision.HIGHEST
product_precision = lax.Precision.HIGH


def inverse_cholesky(inner_gram):
    size = inner_gram.shape[0]
    count = size // 8
    schur = [inner_gram[8 * b:8 * b + 8, :] for b in range(count)]
    rows = lax.broadcasted_iota(jnp.int32, (8, 1), 0)
    cols = lax.broadcasted_iota(jnp.int32, (1, size), 1)
    inverse = [((rows + 8 * b) == cols).astype(jnp.float32) for b in range(count)]
    for j in range(size):
        pivot_block, r = divmod(j, 8)
        pivot_row = schur[pivot_block][r:r + 1, :]
        inv_pivot = lax.rsqrt(pivot_row[:, j:j + 1])
        recip = inv_pivot * inv_pivot
        scaled_row = jnp.where(cols >= j, pivot_row, 0.0) * recip
        inverse_row = inverse[pivot_block][r:r + 1, :]
        for b in range(pivot_block, count):
            col = schur[b][:, j:j + 1]
            if b == pivot_block:
                col = jnp.where(rows >= r, col, 0.0)
                step = jnp.where(rows > r, col * recip, jnp.where(rows == r, 1.0 - inv_pivot, 0.0))
            else:
                step = col * recip
            schur[b] = schur[b] - col * scaled_row
            inverse[b] = inverse[b] - step * inverse_row
    return jnp.concatenate(inverse, axis=0)


def orthonormal_in_kernel(matrix):
    inner_gram = jnp.dot(matrix.T, matrix, precision=highest_precision,
                         preferred_element_type=jnp.float32)
    lower_inverse = inverse_cholesky(inner_gram)
    return lax.dot_general(
        matrix, lower_inverse, (((1,), (1,)), ((), ())), precision=highest_precision,
        preferred_element_type=jnp.float32,
    )


def orthonormal_kernel(block_ref, basis_ref):
    basis_ref[...] = orthonormal_in_kernel(block_ref[...])


def iterate_kernel(packed_ref, basis_ref, out_ref, gram_ref):
    half = packed_ref.shape[1]
    triangles = packed_ref[0:half, :]
    upper_right = packed_ref[half:2 * half, :]
    diagonal = packed_ref[2 * half:2 * half + 1, :]
    rows = lax.broadcasted_iota(jnp.int32, (half, 1), 0)
    cols = lax.broadcasted_iota(jnp.int32, (1, half), 1)
    mirrored = triangles.T
    gram_ref[0:half, 0:half] = jnp.where(rows <= cols, triangles, mirrored)
    lower_right = jnp.where(rows > cols, triangles, mirrored)
    gram_ref[half:, half:] = jnp.where(rows == cols, diagonal, lower_right)
    gram_ref[0:half, half:] = upper_right
    gram_ref[half:, 0:half] = upper_right.T
    basis = basis_ref[...]
    for iteration in range(ITERS - 1):
        product = jnp.dot(gram_ref[...], basis, precision=product_precision,
                          preferred_element_type=jnp.float32)
        basis = orthonormal_in_kernel(product)
    product = jnp.dot(gram_ref[...], basis, precision=product_precision,
                      preferred_element_type=jnp.float32)
    inner_gram = jnp.dot(product.T, product, precision=highest_precision,
                         preferred_element_type=jnp.float32)
    out_ref[...] = lax.dot_general(
        inverse_cholesky(inner_gram), product, (((1,), (1,)), ((), ())),
        precision=highest_precision, preferred_element_type=jnp.float32,
    )


def orthonormal(matrix):
    return pl.pallas_call(
        orthonormal_kernel,
        out_shape=jax.ShapeDtypeStruct(matrix.shape, jnp.float32),
    )(matrix)


def subspace_iteration(packed_gram, mode_basis):
    size = 2 * packed_gram.shape[1]
    return pl.pallas_call(
        iterate_kernel,
        out_shape=jax.ShapeDtypeStruct(mode_basis.shape[::-1], jnp.float32),
        scratch_shapes=[pltpu.VMEM((size, size), jnp.float32)],
    )(packed_gram, mode_basis)


def exchange(blocks, axis):
    return lax.all_to_all(blocks, axis, 0, 0, tiled=True)


def reduce_scatter(matrix, axis):
    parts = lax.axis_size(axis)
    blocks = matrix.reshape(parts, matrix.shape[0] // parts, *matrix.shape[1:])
    return exchange(blocks, axis).sum(0)


def gather(matrix, axis):
    parts = lax.axis_size(axis)
    blocks = jnp.broadcast_to(matrix[None], (parts,) + matrix.shape)
    return exchange(blocks, axis).reshape(parts * matrix.shape[0], *matrix.shape[1:])


def pad_rows(matrix, rows):
    return jnp.pad(matrix, ((0, rows - matrix.shape[0]), (0, 0)))


def all_reduce(matrix):
    groups, fibres = lax.axis_size("group"), lax.axis_size("fibre")
    chunk = -(-matrix.shape[0] // groups)
    rows = pad_rows(matrix, -(-chunk // 8) * 8 * groups)
    rows = reduce_scatter(rows, "group")
    chunk = rows.shape[0]
    rows = pad_rows(rows, -(-chunk // fibres) * fibres)
    rows = reduce_scatter(rows, "fibre")
    rows = gather(rows, "fibre")[:chunk]
    return gather(rows, "group")


def packed_gram_of(fibres, total_columns):
    half = fibres.shape[0] // 2
    top, bottom = fibres[:half], fibres[half:]
    upper_left = jnp.dot(top, top.T, precision=product_precision) / total_columns
    upper_right = jnp.dot(top, bottom.T, precision=product_precision) / total_columns
    lower_right = jnp.dot(bottom, bottom.T, precision=product_precision) / total_columns
    index = jnp.arange(half)
    on_or_above = index[:, None] <= index[None, :]
    triangles = jnp.where(on_or_above, upper_left, lower_right)
    on_diagonal = index[:, None] == index[None, :]
    diagonal = jnp.sum(jnp.where(on_diagonal, lower_right, 0.0), axis=0, keepdims=True)
    return jnp.concatenate([triangles, upper_right, diagonal], axis=0)


def on_device(species_field, start_block):
    fibres = lax.all_to_all(species_field, "fibre", split_axis=1, concat_axis=0, tiled=True)
    total_columns = fibres.shape[1] * lax.axis_size("fibre") * lax.axis_size("group")
    fibres, mode_basis = lax.optimization_barrier((fibres, orthonormal(start_block)))
    packed_gram = all_reduce(packed_gram_of(fibres, total_columns))
    basis_rows = subspace_iteration(packed_gram, mode_basis)
    core_tensor = jnp.dot(basis_rows, fibres, precision=product_precision)
    return (basis_rows.T, core_tensor)


def solution(mesh):
    placed = (P("fibre", "group"), P())
    return jax.shard_map(
        on_device,
        mesh=mesh,
        in_specs=placed,
        out_specs=(P(), P(None, ("group", "fibre"))),
        check_vma=False,
    )
```

```python
import jax
import jax.numpy as jnp
from jax import lax
from jax.experimental import pallas as pl
from jax.experimental.pallas import tpu as pltpu
from jax.sharding import PartitionSpec as P

ITERS = 3


highest_precision = lax.Precision.HIGHEST
product_precision = lax.Precision.HIGH


def inverse_cholesky(inner_gram):
    size = inner_gram.shape[0]
    count = size // 8
    schur = [inner_gram[8 * b:8 * b + 8, :] for b in range(count)]
    rows = lax.broadcasted_iota(jnp.int32, (8, 1), 0)
    cols = lax.broadcasted_iota(jnp.int32, (1, size), 1)
    inverse = [((rows + 8 * b) == cols).astype(jnp.float32) for b in range(count)]
    for j in range(size):
        pivot_block, r = divmod(j, 8)
        pivot_row = schur[pivot_block][r:r + 1, :]
        inv_pivot = lax.rsqrt(pivot_row[:, j:j + 1])
        recip = inv_pivot * inv_pivot
        scaled_row = jnp.where(cols >= j, pivot_row, 0.0) * recip
        inverse_row = inverse[pivot_block][r:r + 1, :]
        for b in range(pivot_block, count):
            col = schur[b][:, j:j + 1]
            if b == pivot_block:
                col = jnp.where(rows >= r, col, 0.0)
                step = jnp.where(rows > r, col * recip, jnp.where(rows == r, 1.0 - inv_pivot, 0.0))
            else:
                step = col * recip
            schur[b] = schur[b] - col * scaled_row
            inverse[b] = inverse[b] - step * inverse_row
    return jnp.concatenate(inverse, axis=0)


def orthonormal_in_kernel(matrix):
    inner_gram = jnp.dot(matrix.T, matrix, precision=product_precision,
                         preferred_element_type=jnp.float32)
    lower_inverse = inverse_cholesky(inner_gram)
    return lax.dot_general(
        matrix, lower_inverse, (((1,), (1,)), ((), ())), precision=product_precision,
        preferred_element_type=jnp.float32,
    )


def orthonormal_kernel(block_ref, basis_ref):
    basis_ref[...] = orthonormal_in_kernel(block_ref[...])


def iterate_kernel(packed_ref, basis_ref, out_ref, gram_ref):
    half = packed_ref.shape[1]
    triangles = packed_ref[0:half, :]
    upper_right = packed_ref[half:2 * half, :]
    diagonal = packed_ref[2 * half:2 * half + 1, :]
    rows = lax.broadcasted_iota(jnp.int32, (half, 1), 0)
    cols = lax.broadcasted_iota(jnp.int32, (1, half), 1)
    mirrored = triangles.T
    gram_ref[0:half, 0:half] = jnp.where(rows <= cols, triangles, mirrored)
    lower_right = jnp.where(rows > cols, triangles, mirrored)
    gram_ref[half:, half:] = jnp.where(rows == cols, diagonal, lower_right)
    gram_ref[0:half, half:] = upper_right
    gram_ref[half:, 0:half] = upper_right.T
    basis = basis_ref[...]
    for iteration in range(ITERS - 1):
        product = jnp.dot(gram_ref[...], basis, precision=product_precision,
                          preferred_element_type=jnp.float32)
        basis = orthonormal_in_kernel(product)
    product = jnp.dot(gram_ref[...], basis, precision=product_precision,
                      preferred_element_type=jnp.float32)
    inner_gram = jnp.dot(product.T, product, precision=product_precision,
                         preferred_element_type=jnp.float32)
    out_ref[...] = lax.dot_general(
        inverse_cholesky(inner_gram), product, (((1,), (1,)), ((), ())),
        precision=product_precision, preferred_element_type=jnp.float32,
    )


def orthonormal(matrix):
    return pl.pallas_call(
        orthonormal_kernel,
        out_shape=jax.ShapeDtypeStruct(matrix.shape, jnp.float32),
    )(matrix)


def subspace_iteration(packed_gram, mode_basis):
    size = 2 * packed_gram.shape[1]
    return pl.pallas_call(
        iterate_kernel,
        out_shape=jax.ShapeDtypeStruct(mode_basis.shape[::-1], jnp.float32),
        scratch_shapes=[pltpu.VMEM((size, size), jnp.float32)],
    )(packed_gram, mode_basis)


def exchange(blocks, axis):
    return lax.all_to_all(blocks, axis, 0, 0, tiled=True)


def reduce_scatter(matrix, axis):
    parts = lax.axis_size(axis)
    blocks = matrix.reshape(parts, matrix.shape[0] // parts, *matrix.shape[1:])
    return exchange(blocks, axis).sum(0)


def gather(matrix, axis):
    parts = lax.axis_size(axis)
    blocks = jnp.broadcast_to(matrix[None], (parts,) + matrix.shape)
    return exchange(blocks, axis).reshape(parts * matrix.shape[0], *matrix.shape[1:])


def pad_rows(matrix, rows):
    return jnp.pad(matrix, ((0, rows - matrix.shape[0]), (0, 0)))


def all_reduce(matrix):
    groups, fibres = lax.axis_size("group"), lax.axis_size("fibre")
    chunk = -(-matrix.shape[0] // groups)
    rows = pad_rows(matrix, -(-chunk // 8) * 8 * groups)
    rows = reduce_scatter(rows, "group")
    chunk = rows.shape[0]
    rows = pad_rows(rows, -(-chunk // fibres) * fibres)
    rows = reduce_scatter(rows, "fibre")
    rows = gather(rows, "fibre")[:chunk]
    return gather(rows, "group")


def pack_symmetric(gram):
    half = gram.shape[0] // 2
    upper_left, upper_right, lower_right = gram[:half, :half], gram[:half, half:], gram[half:, half:]
    index = jnp.arange(half)
    on_or_above = index[:, None] <= index[None, :]
    triangles = jnp.where(on_or_above, upper_left, lower_right)
    on_diagonal = index[:, None] == index[None, :]
    diagonal = jnp.sum(jnp.where(on_diagonal, lower_right, 0.0), axis=0, keepdims=True)
    return jnp.concatenate([triangles, upper_right, diagonal], axis=0)


def on_device(species_field, start_block):
    fibres = lax.all_to_all(species_field, "fibre", split_axis=1, concat_axis=0, tiled=True)
    total_columns = fibres.shape[1] * lax.axis_size("fibre") * lax.axis_size("group")
    fibres, mode_basis = lax.optimization_barrier((fibres, orthonormal(start_block)))
    local_gram = jnp.dot(fibres, fibres.T, precision=product_precision) / total_columns
    packed_gram = all_reduce(pack_symmetric(local_gram))
    basis_rows = subspace_iteration(packed_gram, mode_basis)
    core_tensor = jnp.dot(basis_rows, fibres, precision=product_precision)
    return (basis_rows.T, core_tensor)


def solution(mesh):
    placed = (P("fibre", "group"), P())
    return jax.shard_map(
        on_device,
        mesh=mesh,
        in_specs=placed,
        out_specs=(P(), P(None, ("group", "fibre"))),
        check_vma=False,
    )
```
